256 devices in a mesh: dp: 4 (over y_lo, core), ep: 64 (over y_hi, x, z).
Axes of the slice: x: 4, y: 4 (y_hi: 2, y_lo: 2; y = y_hi * 2 + y_lo), z: 8, core: 2. Of those that a mesh axis runs over, the one named last changes fastest.
Arguments:
- tokens: bfloat16 [32768, 2048], P(('dp', 'ep')), may hold values from -6 to 6
- expert_ids: int32 [32768, 6], P(('dp', 'ep')), may hold values from 0 to 63, all different within a row; in each aligned block of 128 rows (0 to 127, 128 to 255, ...) at most 13 rows name the same one
- gate_scales: float32 [32768, 6], P(('dp', 'ep')), may hold values from 0.05 to 0.5
- expert_slot: int32 [64], replicated, may hold values from 0 to 63, each once
- gate_weight: bfloat16 [64, 2048, 1408], P('ep', 'dp'), may hold values from -0.125 to 0.125
- up_weight: bfloat16 [64, 2048, 1408], P('ep', 'dp'), may hold values from -0.125 to 0.125
- down_weight: bfloat16 [64, 1408, 2048], P('ep', None, 'dp'), may hold values from -0.15625 to 0.15625
Outputs:
- mixed: bfloat16 [32768, 2048], P(('dp', 'ep'))
The draws below stay inside these ranges and needn't reach their ends.
Inputs may be any that keep to these rules, and one draw needn't show every extreme that they name: `expert_ids`: among the 128 tokens of one device no expert is chosen by more than 13; the 6 experts of a token differ. `expert_slot`: each expert has exactly one slot.
All inputs are finite; a program needn't handle non-finite values.
Results may differ from the reference program's by a relative error of at most 0.0057.
Values may be sent and summed in bfloat16 or wider, within the bound.
No kernel may reach another device: no remote copies, remote signals or barrier semaphores. Data moves between devices by JAX's collectives and lax.ppermute only.
A program may use at most 128 MiB of HBM per device.

```python
import math
import jax
import jax.numpy as jnp
import numpy as np
from jax import lax

D = 2048
FF = 1408
EXPERTS = 64
TOP = 6
TOK_DEV = 128
C = 13
TOKENS = 32768
N_DP = 4
N_EP = 64


def levels(key, dims, split, smallest, top_value):
    gain, own = 1.0, jax.random.fold_in(key, 6)
    for axis_at, shards_of in split:
        steps = jnp.exp(jax.random.uniform(jax.random.fold_in(own, axis_at), (shards_of,), jnp.float32, smallest / len(split), top_value / len(split)))
        gain = gain * jnp.repeat(steps, dims[axis_at] // shards_of).reshape([-1 if axis == axis_at else 1 for axis in range(len(dims))])
    return gain


def assign_block(own_key, own, number, rows, amount, top, limit, slope):
    ranking = jax.random.permutation(own_key, amount)
    packed, usual = portions_of(amount, rows * top, limit, slope, True), portions_of(amount, rows * top, limit, slope, False)
    places = jnp.arange(amount)

    def named(tallies, turn):
        used = int((tallies > 0).sum())
        fixed = max(1, used // 4)
        moved = fixed + (places - fixed + turn * (used - fixed)) % max(1, amount - fixed)
        return jnp.zeros((amount,), jnp.int32).at[ranking[jnp.where(places < fixed, places, moved)]].set(jnp.asarray(tallies, jnp.int32))

    tallies = jnp.where(number % 4 == 0, named(packed, number // 4), named(usual, number - number // 4 - 1))
    mixed = jax.random.permutation(jax.random.fold_in(own, 3), amount)
    donor, receiver = mixed[0:amount // 2 * 2:2], mixed[1:amount // 2 * 2:2]
    room = jnp.minimum(tallies[donor] - 1, limit - tallies[receiver]) // 2
    room = jnp.where((donor == ranking[0]) | (receiver == ranking[0]) | (tallies[receiver] == 0), 0, jnp.maximum(room, 0))
    moved = jax.random.randint(jax.random.fold_in(own, 4), (amount // 2,), 0, 1 << 20) % (room + 1)
    tallies = tallies.at[donor].add(-moved).at[receiver].add(moved)
    items = jnp.searchsorted(jnp.cumsum(tallies), jnp.arange(rows * top), side="right").astype(jnp.int32)
    listing = items.reshape(top, rows).T
    listing = listing[jax.random.permutation(jax.random.fold_in(own, 1), rows)]
    turn = jax.random.randint(jax.random.fold_in(own, 2), (rows, 1), 0, top)
    return jnp.take_along_axis(listing, (jnp.arange(top)[None, :] + turn) % top, axis=1)


def portions_of(number_of, total, reach, slope, full):
    weights = [(1 << 20) // math.isqrt(grade ** slope) + 1 for grade in range(1, number_of + 1)]
    largest = reach if full else min(reach, max(-(-total // number_of), total * weights[0] // sum(weights)))
    least = 1 if total - largest >= number_of - 1 else 0
    given, rest = [largest] + [least] * (number_of - 1), total - largest - least * (number_of - 1)
    while rest > 0:
        candidates = [i for i in range(1, number_of) if given[i] < largest] or [i for i in range(1, number_of) if given[i] < reach]
        whole, left = sum([weights[i] for i in candidates]), rest
        for i in candidates:
            addition = min(reach - given[i], max(1, left * weights[i] // whole), rest)
            given[i] = given[i] + addition
            rest = rest - addition
    return np.array(given)


def gaussian(own_key, dims, spread, bound, split=(), kind=jnp.bfloat16):
    loudness = levels(own_key, dims, split, -0.22, 0.18) if split else 1.0
    array = jax.random.normal(own_key, dims, jnp.float32) * spread * loudness
    return jnp.minimum(jnp.maximum(array, -bound), bound).astype(kind)


def setup_inputs(seed: int = 0) -> dict:
    key_list = jax.random.split(jax.random.key(seed), 8)
    tokens = gaussian(key_list[0], (TOKENS, D), 1.0, 6.0, ((0, 256),))
    expert_ids_keys = jax.random.split(jax.random.fold_in(key_list[1], 1), TOKENS // TOK_DEV)
    expert_ids_turns = jax.random.permutation(jax.random.fold_in(key_list[1], 3), TOKENS // TOK_DEV)
    expert_ids = jax.vmap(lambda own, number: assign_block(jax.random.fold_in(key_list[1], 2), own, number, TOK_DEV, EXPERTS, TOP, C, 1))(expert_ids_keys, expert_ids_turns).reshape((TOKENS, TOP))
    gate_scales = jnp.clip(jnp.exp(math.log(0.5) - 2.3025851 * jax.random.uniform(key_list[2], (TOKENS, TOP), jnp.float32) ** levels(key_list[2], (TOKENS, TOP), ((0, 256),), -0.2, 0.2)), 0.05, 0.5)
    expert_slot = jax.random.permutation(key_list[3], EXPERTS).astype(jnp.int32)
    gate_weight = gaussian(key_list[4], (EXPERTS, D, FF), D ** -0.5, 0.125, ((0, 64), (1, 4)))
    up_weight = gaussian(key_list[5], (EXPERTS, D, FF), D ** -0.5, 0.125, ((0, 64), (1, 4)))
    down_weight = gaussian(key_list[6], (EXPERTS, FF, D), FF ** -0.5, 0.15625, ((0, 64), (2, 4)))
    return dict(tokens=tokens, expert_ids=expert_ids, gate_scales=gate_scales, expert_slot=expert_slot, gate_weight=gate_weight, up_weight=up_weight, down_weight=down_weight)


def reference(tokens, expert_ids, gate_scales, expert_slot, gate_weight, up_weight, down_weight):
    total = TOKENS * TOP
    ids = expert_ids.reshape(-1).astype(jnp.int32)
    scales = gate_scales.reshape(-1).astype(jnp.float32)
    order = jnp.argsort(ids, stable=True).astype(jnp.int32)
    counts = jnp.sum((ids[:, None] == jnp.arange(EXPERTS, dtype=jnp.int32)[None, :]).astype(jnp.int32), 0)
    starts = (jnp.cumsum(counts) - counts).astype(jnp.int32)
    width = N_DP * N_EP * C
    offsets = jnp.arange(width, dtype=jnp.int32)

    def one_expert(mixed, expert):
        position = jnp.minimum(starts[expert] + offsets, total - 1).astype(jnp.int32)
        valid = offsets < counts[expert]
        chosen = order[position]
        rows = chosen // TOP
        picked = tokens[rows]
        slot = expert_slot[expert]
        gate = jnp.dot(picked, gate_weight[slot], preferred_element_type=jnp.float32)
        up = jnp.dot(picked, up_weight[slot], preferred_element_type=jnp.float32)
        hidden = (jax.nn.silu(gate) * up).astype(jnp.bfloat16)
        output = jnp.dot(hidden, down_weight[slot], preferred_element_type=jnp.float32).astype(jnp.bfloat16)
        weight = jnp.where(valid, scales[chosen], jnp.zeros_like(scales[chosen]))
        mixed = mixed.at[rows].add(weight[:, None] * output.astype(jnp.float32))
        return mixed, None

    start = jnp.zeros((TOKENS, D), jnp.float32)
    mixed, _ = lax.scan(one_expert, start, jnp.arange(EXPERTS, dtype=jnp.int32))
    return mixed.astype(jnp.bfloat16)
```

```python
import jax
import jax.numpy as jnp
from jax import lax
from jax.sharding import PartitionSpec as P

C = 13
OFFS = (0, 2, 1, 3)


def _perm(n, m):
    return [(i, i ^ m) for i in range(n)]


def _dp_gather(ws, axis):
    n = lax.axis_size("dp")
    cross = lax.ppermute(ws, "dp", _perm(n, 2))
    near = lax.ppermute(ws, "dp", _perm(n, 1))
    far = lax.ppermute(cross, "dp", _perm(n, 1))
    return [jnp.concatenate(parts, axis=axis) for parts in zip(ws, cross, near, far)]


def _blocks(x, idx):
    rows, width = x.shape
    nb = idx.shape[0]
    return jnp.take(x.reshape(rows, nb, width // nb), idx, axis=1).reshape(rows, width)


def local(tokens, expert_ids, gate_scales, expert_slot, gate_weight, up_weight, down_weight):
    tok_rows, width = tokens.shape
    top = expert_ids.shape[1]
    experts = expert_slot.shape[0]
    n_ep = lax.axis_size("ep")
    n_dp = lax.axis_size("dp")
    assert n_dp == len(OFFS) and gate_weight.shape[0] == 1 and experts == n_ep
    cap = C
    slots = experts * cap

    wg, wu = _dp_gather((gate_weight[0], up_weight[0]), 0)
    (wd,) = _dp_gather((down_weight[0],), 1)

    d = lax.axis_index("dp")
    offs = jnp.array(OFFS, jnp.int32)
    src_blk = d ^ offs
    inv = jnp.argsort(offs).astype(jnp.int32)
    out_blk = inv[d ^ jnp.arange(n_dp, dtype=jnp.int32)]

    ids = expert_ids.reshape(-1)
    onehot = (ids[:, None] == jnp.arange(experts, dtype=jnp.int32)[None, :]).astype(jnp.int32)
    rank = jnp.sum((jnp.cumsum(onehot, 0) - onehot) * onehot, 1)
    target = jnp.sum(onehot * expert_slot[None, :], 1)
    flat = (target * cap + rank).reshape(tok_rows, top)

    rows_j = jnp.arange(slots, dtype=jnp.int32)
    pick = jnp.any(flat[None, :, :] == rows_j[:, None, None], axis=2).astype(jnp.bfloat16)
    tokens_rel = _blocks(tokens, src_blk)
    send = jnp.dot(pick, tokens_rel, preferred_element_type=jnp.float32).astype(jnp.bfloat16)
    received = lax.all_to_all(send.reshape(n_ep, 1, cap, width), "ep", 0, 0, tiled=True)
    received = received.reshape(slots, width)

    gate = jnp.dot(received, wg, preferred_element_type=jnp.float32)
    up = jnp.dot(received, wu, preferred_element_type=jnp.float32)
    hidden = (jax.nn.silu(gate) * up).astype(jnp.bfloat16)
    expert_out = jnp.dot(hidden, wd, preferred_element_type=jnp.float32).astype(jnp.bfloat16)

    returned = lax.all_to_all(expert_out.reshape(n_ep, 1, cap, width), "ep", 0, 0, tiled=True)
    returned = returned.reshape(slots, width)

    hit = flat[:, :, None] == rows_j[None, None, :]
    weights = jnp.sum(jnp.where(hit, gate_scales[:, :, None], 0.0), axis=1)
    w_hi = weights.astype(jnp.bfloat16)
    w_lo = (weights - w_hi.astype(jnp.float32)).astype(jnp.bfloat16)
    mixed = jnp.dot(w_hi, returned, preferred_element_type=jnp.float32)
    mixed = mixed + jnp.dot(w_lo, returned, preferred_element_type=jnp.float32)
    return _blocks(mixed.astype(jnp.bfloat16), out_blk)


def solution(mesh):
    in_specs = (
        P(("dp", "ep"), None),
        P(("dp", "ep"), None),
        P(("dp", "ep"), None),
        P(),
        P("ep", "dp", None),
        P("ep", "dp", None),
        P("ep", None, "dp"),
    )
    out_specs = P(("dp", "ep"), None)
    return jax.shard_map(local, mesh=mesh, in_specs=in_specs, out_specs=out_specs, check_vma=False)
```

```python
import jax
import jax.numpy as jnp
from jax import lax
from jax.sharding import PartitionSpec as P

C = 13
OFFS = (0, 2, 1, 3)


def _perm(n, m):
    return [(i, i ^ m) for i in range(n)]


def _dp_gather(ws, axis):
    n = lax.axis_size("dp")
    cross = lax.ppermute(ws, "dp", _perm(n, 2))
    near = lax.ppermute(ws, "dp", _perm(n, 1))
    far = lax.ppermute(cross, "dp", _perm(n, 1))
    return [jnp.concatenate(parts, axis=axis) for parts in zip(ws, cross, near, far)]


def _blocks(x, idx):
    rows, width = x.shape
    nb = idx.shape[0]
    return jnp.take(x.reshape(rows, nb, width // nb), idx, axis=1).reshape(rows, width)


def local(tokens, expert_ids, gate_scales, expert_slot, gate_weight, up_weight, down_weight):
    tok_rows, width = tokens.shape
    top = expert_ids.shape[1]
    experts = expert_slot.shape[0]
    n_ep = lax.axis_size("ep")
    n_dp = lax.axis_size("dp")
    assert n_dp == len(OFFS) and gate_weight.shape[0] == 1 and experts == n_ep
    cap = C
    slots = experts * cap

    wg, wu = _dp_gather((gate_weight[0], up_weight[0]), 0)
    down_shard = lax.optimization_barrier((down_weight[0], wg, wu))[0]
    (wd,) = _dp_gather((down_shard,), 1)

    d = lax.axis_index("dp")
    offs = jnp.array(OFFS, jnp.int32)
    src_blk = d ^ offs
    inv = jnp.argsort(offs).astype(jnp.int32)
    out_blk = inv[d ^ jnp.arange(n_dp, dtype=jnp.int32)]

    ids = expert_ids.reshape(-1)
    onehot = (ids[:, None] == jnp.arange(experts, dtype=jnp.int32)[None, :]).astype(jnp.int32)
    rank = jnp.sum((jnp.cumsum(onehot, 0) - onehot) * onehot, 1)
    target = jnp.sum(onehot * expert_slot[None, :], 1)
    flat = (target * cap + rank).reshape(tok_rows, top)

    rows_j = jnp.arange(slots, dtype=jnp.int32)
    pick = jnp.any(flat[None, :, :] == rows_j[:, None, None], axis=2).astype(jnp.bfloat16)
    lanes = 128
    sub = width // lanes
    tokens_rel = _blocks(tokens, src_blk).reshape(tok_rows, sub, lanes)
    send = jnp.einsum("st,trl->srl", pick, tokens_rel, preferred_element_type=jnp.float32)
    send = send.astype(jnp.bfloat16).reshape(n_ep, cap * sub, lanes)
    received = lax.all_to_all(send, "ep", 0, 0, tiled=True)
    received = received.reshape(slots, width)

    gate = jnp.dot(received, wg, preferred_element_type=jnp.float32)
    up = jnp.dot(received, wu, preferred_element_type=jnp.float32)
    hidden = (jax.nn.silu(gate) * up).astype(jnp.bfloat16)
    expert_out = jnp.dot(hidden, wd, preferred_element_type=jnp.float32).astype(jnp.bfloat16)

    expert_out = expert_out.reshape(n_ep, cap * sub, lanes)
    returned = lax.all_to_all(expert_out, "ep", 0, 0, tiled=True)
    returned = returned.reshape(slots, sub, lanes)

    hit = flat[:, :, None] == rows_j[None, None, :]
    weights = jnp.sum(jnp.where(hit, gate_scales[:, :, None], 0.0), axis=1)
    w_hi32 = lax.reduce_precision(weights, exponent_bits=8, mantissa_bits=7)
    w_hi = w_hi32.astype(jnp.bfloat16)
    w_lo = (weights - w_hi32).astype(jnp.bfloat16)
    mixed = jnp.einsum("ts,srl->trl", w_hi, returned, preferred_element_type=jnp.float32)
    mixed = mixed + jnp.einsum("ts,srl->trl", w_lo, returned, preferred_element_type=jnp.float32)
    return _blocks(mixed.astype(jnp.bfloat16).reshape(tok_rows, width), out_blk)


def solution(mesh):
    in_specs = (
        P(("dp", "ep"), None),
        P(("dp", "ep"), None),
        P(("dp", "ep"), None),
        P(),
        P("ep", "dp", None),
        P("ep", "dp", None),
        P("ep", None, "dp"),
    )
    out_specs = P(("dp", "ep"), None)
    return jax.shard_map(local, mesh=mesh, in_specs=in_specs, out_specs=out_specs, check_vma=False)
```

```python
import jax
import jax.numpy as jnp
from jax import lax
from jax.sharding import PartitionSpec as P

C = 13
OFFS = (0, 2, 1, 3)


def _perm(n, m):
    return [(i, i ^ m) for i in range(n)]


def _dp_parts(w):
    n = lax.axis_size("dp")
    cross = lax.ppermute(w, "dp", _perm(n, 2))
    near = lax.ppermute(w, "dp", _perm(n, 1))
    far = lax.ppermute(cross, "dp", _perm(n, 1))
    return [w, cross, near, far]


def _blocks(x, idx):
    rows, width = x.shape
    nb = idx.shape[0]
    return jnp.take(x.reshape(rows, nb, width // nb), idx, axis=1).reshape(rows, width)


def local(tokens, expert_ids, gate_scales, expert_slot, gate_weight, up_weight, down_weight):
    tok_rows, width = tokens.shape
    top = expert_ids.shape[1]
    experts = expert_slot.shape[0]
    n_ep = lax.axis_size("ep")
    n_dp = lax.axis_size("dp")
    assert n_dp == len(OFFS) and gate_weight.shape[0] == 1 and experts == n_ep
    cap = C
    slots = experts * cap

    wg = _dp_parts(gate_weight[0])
    up_shard = lax.optimization_barrier((up_weight[0], wg[1]))[0]
    wu = _dp_parts(up_shard)
    down_shard = lax.optimization_barrier((down_weight[0], wu[1]))[0]
    wd = _dp_parts(down_shard)

    d = lax.axis_index("dp")
    offs = jnp.array(OFFS, jnp.int32)
    src_blk = d ^ offs
    inv = jnp.argsort(offs).astype(jnp.int32)
    out_blk = inv[d ^ jnp.arange(n_dp, dtype=jnp.int32)]

    ids = expert_ids.reshape(-1)
    onehot = (ids[:, None] == jnp.arange(experts, dtype=jnp.int32)[None, :]).astype(jnp.int32)
    rank = jnp.sum((jnp.cumsum(onehot, 0) - onehot) * onehot, 1)
    target = jnp.sum(onehot * expert_slot[None, :], 1)
    flat = (target * cap + rank).reshape(tok_rows, top)

    rows_j = jnp.arange(slots, dtype=jnp.int32)
    pick = jnp.any(flat[None, :, :] == rows_j[:, None, None], axis=2).astype(jnp.bfloat16)
    lanes = 128
    sub = width // lanes
    tokens_rel = _blocks(tokens, src_blk).reshape(tok_rows, sub, lanes)
    send = jnp.einsum("st,trl->srl", pick, tokens_rel, preferred_element_type=jnp.float32)
    send = send.astype(jnp.bfloat16).reshape(n_ep, cap * sub, lanes)
    received = lax.all_to_all(send, "ep", 0, 0, tiled=True)
    received = received.reshape(slots, width)

    kb = width // n_dp
    cols = [received[:, p * kb:(p + 1) * kb] for p in range(n_dp)]
    gate = sum(jnp.dot(c, w, preferred_element_type=jnp.float32) for c, w in zip(cols, wg))
    up = sum(jnp.dot(c, w, preferred_element_type=jnp.float32) for c, w in zip(cols, wu))
    hidden = (jax.nn.silu(gate) * up).astype(jnp.bfloat16)
    outs = [jnp.dot(hidden, w, preferred_element_type=jnp.float32).astype(jnp.bfloat16) for w in wd]
    expert_out = jnp.concatenate(outs, axis=1)

    expert_out = expert_out.reshape(n_ep, cap * sub, lanes)
    returned = lax.all_to_all(expert_out, "ep", 0, 0, tiled=True)
    returned = returned.reshape(slots, sub, lanes)

    hit = flat[:, :, None] == rows_j[None, None, :]
    weights = jnp.sum(jnp.where(hit, gate_scales[:, :, None], 0.0), axis=1)
    w_hi32 = lax.reduce_precision(weights, exponent_bits=8, mantissa_bits=7)
    w_hi = w_hi32.astype(jnp.bfloat16)
    w_lo = (weights - w_hi32).astype(jnp.bfloat16)
    mixed = jnp.einsum("ts,srl->trl", w_hi, returned, preferred_element_type=jnp.float32)
    mixed = mixed + jnp.einsum("ts,srl->trl", w_lo, returned, preferred_element_type=jnp.float32)
    return _blocks(mixed.astype(jnp.bfloat16).reshape(tok_rows, width), out_blk)


def solution(mesh):
    in_specs = (
        P(("dp", "ep"), None),
        P(("dp", "ep"), None),
        P(("dp", "ep"), None),
        P(),
        P("ep", "dp", None),
        P("ep", "dp", None),
        P("ep", None, "dp"),
    )
    out_specs = P(("dp", "ep"), None)
    return jax.shard_map(local, mesh=mesh, in_specs=in_specs, out_specs=out_specs, check_vma=False)
```

```python
import jax
import jax.numpy as jnp
from jax import lax
from jax.sharding import PartitionSpec as P

C = 13
OFFS = (0, 2, 1, 3)


def _perm(n, m):
    return [(i, i ^ m) for i in range(n)]


def _dp_parts(w):
    n = lax.axis_size("dp")
    cross = lax.ppermute(w, "dp", _perm(n, 2))
    near = lax.ppermute(w, "dp", _perm(n, 1))
    far = lax.ppermute(cross, "dp", _perm(n, 1))
    return [w, cross, near, far]


def _blocks(x, idx):
    rows, width = x.shape
    nb = idx.shape[0]
    return jnp.take(x.reshape(rows, nb, width // nb), idx, axis=1).reshape(rows, width)


def local(tokens, expert_ids, gate_scales, expert_slot, gate_weight, up_weight, down_weight):
    tok_rows, width = tokens.shape
    top = expert_ids.shape[1]
    experts = expert_slot.shape[0]
    n_ep = lax.axis_size("ep")
    n_dp = lax.axis_size("dp")
    assert n_dp == len(OFFS) and gate_weight.shape[0] == 1 and experts == n_ep
    cap = C
    slots = experts * cap

    wg = _dp_parts(gate_weight[0])
    up_shard = lax.optimization_barrier((up_weight[0], wg[1]))[0]
    wu = _dp_parts(up_shard)
    wg = jnp.concatenate(wg, axis=0)
    down_shard = lax.optimization_barrier((down_weight[0], wu[1], wg))[0]
    wd = _dp_parts(down_shard)
    wu = jnp.concatenate(wu, axis=0)
    wd = jnp.concatenate(wd, axis=1)

    d = lax.axis_index("dp")
    offs = jnp.array(OFFS, jnp.int32)
    src_blk = d ^ offs
    inv = jnp.argsort(offs).astype(jnp.int32)
    out_blk = inv[d ^ jnp.arange(n_dp, dtype=jnp.int32)]

    ids = expert_ids.reshape(-1)
    onehot = (ids[:, None] == jnp.arange(experts, dtype=jnp.int32)[None, :]).astype(jnp.int32)
    rank = jnp.sum((jnp.cumsum(onehot, 0) - onehot) * onehot, 1)
    target = jnp.sum(onehot * expert_slot[None, :], 1)
    flat = (target * cap + rank).reshape(tok_rows, top)

    rows_j = jnp.arange(slots, dtype=jnp.int32)
    pick = jnp.any(flat[None, :, :] == rows_j[:, None, None], axis=2).astype(jnp.bfloat16)
    lanes = 128
    sub = width // lanes
    tokens_rel = _blocks(tokens, src_blk).reshape(tok_rows, sub, lanes)
    send = jnp.einsum("st,trl->srl", pick, tokens_rel, preferred_element_type=jnp.float32)
    send = send.astype(jnp.bfloat16).reshape(n_ep, cap * sub, lanes)
    received = lax.all_to_all(send, "ep", 0, 0, tiled=True)
    received = received.reshape(slots, width)

    gate = jnp.dot(received, wg, preferred_element_type=jnp.float32)
    up = jnp.dot(received, wu, preferred_element_type=jnp.float32)
    hidden = (jax.nn.silu(gate) * up).astype(jnp.bfloat16)
    expert_out = jnp.dot(hidden, wd, preferred_element_type=jnp.float32).astype(jnp.bfloat16)

    expert_out = expert_out.reshape(n_ep, cap * sub, lanes)
    returned = lax.all_to_all(expert_out, "ep", 0, 0, tiled=True)
    returned = returned.reshape(slots, sub, lanes)

    hit = flat[:, :, None] == rows_j[None, None, :]
    weights = jnp.sum(jnp.where(hit, gate_scales[:, :, None], 0.0), axis=1)
    w_hi32 = lax.reduce_precision(weights, exponent_bits=8, mantissa_bits=7)
    w_hi = w_hi32.astype(jnp.bfloat16)
    w_lo = (weights - w_hi32).astype(jnp.bfloat16)
    mixed = jnp.einsum("ts,srl->trl", w_hi, returned, preferred_element_type=jnp.float32)
    mixed = mixed + jnp.einsum("ts,srl->trl", w_lo, returned, preferred_element_type=jnp.float32)
    return _blocks(mixed.astype(jnp.bfloat16).reshape(tok_rows, width), out_blk)


def solution(mesh):
    in_specs = (
        P(("dp", "ep"), None),
        P(("dp", "ep"), None),
        P(("dp", "ep"), None),
        P(),
        P("ep", "dp", None),
        P("ep", "dp", None),
        P("ep", None, "dp"),
    )
    out_specs = P(("dp", "ep"), None)
    return jax.shard_map(local, mesh=mesh, in_specs=in_specs, out_specs=out_specs, check_vma=False)
```

```python
import jax
import jax.numpy as jnp
from jax import lax
from jax.sharding import PartitionSpec as P

C = 13
OFFS = (0, 2, 1, 3)


def _perm(n, m):
    return [(i, i ^ m) for i in range(n)]


def _dp_parts(w, after=None):
    n = lax.axis_size("dp")
    cross = lax.ppermute(w, "dp", _perm(n, 2))
    near = lax.ppermute(w, "dp", _perm(n, 1))
    relay = cross if after is None else lax.optimization_barrier((cross, after()))[0]
    far = lax.ppermute(relay, "dp", _perm(n, 1))
    return [w, cross, near, far]


def _blocks(x, idx):
    rows, width = x.shape
    nb = idx.shape[0]
    return jnp.take(x.reshape(rows, nb, width // nb), idx, axis=1).reshape(rows, width)


def local(tokens, expert_ids, gate_scales, expert_slot, gate_weight, up_weight, down_weight):
    tok_rows, width = tokens.shape
    top = expert_ids.shape[1]
    experts = expert_slot.shape[0]
    n_ep = lax.axis_size("ep")
    n_dp = lax.axis_size("dp")
    assert n_dp == len(OFFS) and gate_weight.shape[0] == 1 and experts == n_ep
    cap = C
    slots = experts * cap

    wg = _dp_parts(gate_weight[0])
    up_shard = lax.optimization_barrier((up_weight[0], wg[1]))[0]
    wu = _dp_parts(up_shard)
    gate_cross = wg[1]
    wg = jnp.concatenate(wg, axis=0)
    down_shard = lax.optimization_barrier((down_weight[0], wu[1], wg))[0]
    wu = jnp.concatenate(wu, axis=0)

    d = lax.axis_index("dp")
    offs = jnp.array(OFFS, jnp.int32)
    src_blk = d ^ offs
    inv = jnp.argsort(offs).astype(jnp.int32)
    out_blk = inv[d ^ jnp.arange(n_dp, dtype=jnp.int32)]

    ids = expert_ids.reshape(-1)
    onehot = (ids[:, None] == jnp.arange(experts, dtype=jnp.int32)[None, :]).astype(jnp.int32)
    rank = jnp.sum((jnp.cumsum(onehot, 0) - onehot) * onehot, 1)
    target = jnp.sum(onehot * expert_slot[None, :], 1)
    flat = (target * cap + rank).reshape(tok_rows, top)

    rows_j = jnp.arange(slots, dtype=jnp.int32)
    pick = jnp.any(flat[None, :, :] == rows_j[:, None, None], axis=2).astype(jnp.bfloat16)
    lanes = 128
    sub = width // lanes
    tokens_rel = _blocks(tokens, src_blk).reshape(tok_rows, sub, lanes)
    send = jnp.einsum("st,trl->srl", pick, tokens_rel, preferred_element_type=jnp.float32)
    send = send.astype(jnp.bfloat16).reshape(n_ep, cap * sub, lanes)
    send = lax.optimization_barrier((send, gate_cross))[0]
    received = lax.all_to_all(send, "ep", 0, 0, tiled=True)
    received = received.reshape(slots, width)

    gate = jnp.dot(received, wg, preferred_element_type=jnp.float32)
    wd = jnp.concatenate(_dp_parts(down_shard, after=lambda: gate), axis=1)
    up = jnp.dot(received, wu, preferred_element_type=jnp.float32)
    hidden = (jax.nn.silu(gate) * up).astype(jnp.bfloat16)
    expert_out = jnp.dot(hidden, wd, preferred_element_type=jnp.float32).astype(jnp.bfloat16)

    expert_out = expert_out.reshape(n_ep, cap * sub, lanes)
    returned = lax.all_to_all(expert_out, "ep", 0, 0, tiled=True)
    returned = returned.reshape(slots, sub, lanes)

    hit = flat[:, :, None] == rows_j[None, None, :]
    weights = jnp.sum(jnp.where(hit, gate_scales[:, :, None], 0.0), axis=1)
    w_hi32 = lax.reduce_precision(weights, exponent_bits=8, mantissa_bits=7)
    w_hi = w_hi32.astype(jnp.bfloat16)
    w_lo = (weights - w_hi32).astype(jnp.bfloat16)
    mixed = jnp.einsum("ts,srl->trl", w_hi, returned, preferred_element_type=jnp.float32)
    mixed = mixed + jnp.einsum("ts,srl->trl", w_lo, returned, preferred_element_type=jnp.float32)
    return _blocks(mixed.astype(jnp.bfloat16).reshape(tok_rows, width), out_blk)


def solution(mesh):
    in_specs = (
        P(("dp", "ep"), None),
        P(("dp", "ep"), None),
        P(("dp", "ep"), None),
        P(),
        P("ep", "dp", None),
        P("ep", "dp", None),
        P("ep", None, "dp"),
    )
    out_specs = P(("dp", "ep"), None)
    return jax.shard_map(local, mesh=mesh, in_specs=in_specs, out_specs=out_specs, check_vma=False)
```

```python
import jax
import jax.numpy as jnp
from jax import lax
from jax.sharding import PartitionSpec as P

C = 13
OFFS = (0, 2, 1, 3)


def _perm(n, m):
    return [(i, i ^ m) for i in range(n)]


def _dp_parts(w, after=None):
    n = lax.axis_size("dp")
    cross = lax.ppermute(w, "dp", _perm(n, 2))
    near = lax.ppermute(w, "dp", _perm(n, 1))
    relay = cross if after is None else lax.optimization_barrier((cross, after()))[0]
    far = lax.ppermute(relay, "dp", _perm(n, 1))
    return [w, cross, near, far]


def _blocks(x, idx):
    rows, width = x.shape
    nb = idx.shape[0]
    return jnp.take(x.reshape(rows, nb, width // nb), idx, axis=1).reshape(rows, width)


def local(tokens, expert_ids, gate_scales, expert_slot, gate_weight, up_weight, down_weight):
    tok_rows, width = tokens.shape
    top = expert_ids.shape[1]
    experts = expert_slot.shape[0]
    n_ep = lax.axis_size("ep")
    n_dp = lax.axis_size("dp")
    assert n_dp == len(OFFS) and gate_weight.shape[0] == 1 and experts == n_ep
    cap = C
    slots = experts * cap

    wg = _dp_parts(gate_weight[0])
    up_shard = lax.optimization_barrier((up_weight[0], wg[1]))[0]
    wu = _dp_parts(up_shard)
    gate_cross = wg[1]
    wg = jnp.concatenate(wg, axis=0)
    down_shard = lax.optimization_barrier((down_weight[0], wu[1], wg))[0]
    wu = jnp.concatenate(wu, axis=0)

    d = lax.axis_index("dp")
    offs = jnp.array(OFFS, jnp.int32)
    src_blk = d ^ offs
    inv = jnp.argsort(offs).astype(jnp.int32)
    out_blk = inv[d ^ jnp.arange(n_dp, dtype=jnp.int32)]

    ids = expert_ids.reshape(-1)
    onehot = (ids[:, None] == jnp.arange(experts, dtype=jnp.int32)[None, :]).astype(jnp.int32)
    rank = jnp.sum((jnp.cumsum(onehot, 0) - onehot) * onehot, 1)
    target = jnp.sum(onehot * expert_slot[None, :], 1)
    flat = (target * cap + rank).reshape(tok_rows, top)

    rows_j = jnp.arange(slots, dtype=jnp.int32)
    pick = jnp.any(flat[None, :, :] == rows_j[:, None, None], axis=2).astype(jnp.bfloat16)
    lanes = 128
    sub = width // lanes
    tokens_rel = _blocks(tokens, src_blk).reshape(tok_rows, sub, lanes)
    send = jnp.einsum("st,trl->srl", pick, tokens_rel, preferred_element_type=jnp.float32)
    send = send.astype(jnp.bfloat16).reshape(n_ep, cap * sub, lanes)
    send = lax.optimization_barrier((send, gate_cross))[0]
    received = lax.all_to_all(send, "ep", 0, 0, tiled=True)
    received = received.reshape(slots, width)

    gate = jnp.dot(received, wg, preferred_element_type=jnp.float32)
    up = jnp.dot(received, wu, preferred_element_type=jnp.float32)
    hidden = (jax.nn.silu(gate) * up).astype(jnp.bfloat16)
    wd = jnp.concatenate(_dp_parts(down_shard, after=lambda: hidden), axis=1)
    expert_out = jnp.dot(hidden, wd, preferred_element_type=jnp.float32).astype(jnp.bfloat16)

    expert_out = expert_out.reshape(n_ep, cap * sub, lanes)
    returned = lax.all_to_all(expert_out, "ep", 0, 0, tiled=True)
    returned = returned.reshape(slots, sub, lanes)

    hit = flat[:, :, None] == rows_j[None, None, :]
    weights = jnp.sum(jnp.where(hit, gate_scales[:, :, None], 0.0), axis=1)
    w_hi32 = lax.reduce_precision(weights, exponent_bits=8, mantissa_bits=7)
    w_hi = w_hi32.astype(jnp.bfloat16)
    w_lo = (weights - w_hi32).astype(jnp.bfloat16)
    both = jnp.einsum("ts,srl->trl", jnp.concatenate([w_hi, w_lo], axis=0), returned,
                      preferred_element_type=jnp.float32)
    mixed = both[:tok_rows] + both[tok_rows:]
    return _blocks(mixed.astype(jnp.bfloat16).reshape(tok_rows, width), out_blk)


def solution(mesh):
    in_specs = (
        P(("dp", "ep"), None),
        P(("dp", "ep"), None),
        P(("dp", "ep"), None),
        P(),
        P("ep", "dp", None),
        P("ep", "dp", None),
        P("ep", None, "dp"),
    )
    out_specs = P(("dp", "ep"), None)
    return jax.shard_map(local, mesh=mesh, in_specs=in_specs, out_specs=out_specs, check_vma=False)
```

```python
import jax
import jax.numpy as jnp
from jax import lax
from jax.sharding import PartitionSpec as P

C = 13
OFFS = (0, 2, 1, 3)


def _perm(n, m):
    return [(i, i ^ m) for i in range(n)]


def _dp_parts(w, after=None):
    n = lax.axis_size("dp")
    cross = lax.ppermute(w, "dp", _perm(n, 2))
    near = lax.ppermute(w, "dp", _perm(n, 1))
    relay = cross if after is None else lax.optimization_barrier((cross, after()))[0]
    far = lax.ppermute(relay, "dp", _perm(n, 1))
    return [w, cross, near, far]


def _blocks(x, idx):
    rows, width = x.shape
    nb = idx.shape[0]
    return jnp.take(x.reshape(rows, nb, width // nb), idx, axis=1).reshape(rows, width)


def local(tokens, expert_ids, gate_scales, expert_slot, gate_weight, up_weight, down_weight):
    tok_rows, width = tokens.shape
    top = expert_ids.shape[1]
    experts = expert_slot.shape[0]
    n_ep = lax.axis_size("ep")
    n_dp = lax.axis_size("dp")
    assert n_dp == len(OFFS) and gate_weight.shape[0] == 1 and experts == n_ep
    cap = C
    slots = experts * cap

    wg = _dp_parts(gate_weight[0])
    up_shard = lax.optimization_barrier((up_weight[0], wg[1]))[0]
    wu = _dp_parts(up_shard)
    gate_cross = wg[1]
    wg = jnp.concatenate(wg, axis=0)
    down_shard = lax.optimization_barrier((down_weight[0], wu[1]))[0]
    wu = jnp.concatenate(wu, axis=0)

    d = lax.axis_index("dp")
    offs = jnp.array(OFFS, jnp.int32)
    src_blk = d ^ offs
    inv = jnp.argsort(offs).astype(jnp.int32)
    out_blk = inv[d ^ jnp.arange(n_dp, dtype=jnp.int32)]

    ids = expert_ids.reshape(-1)
    onehot = (ids[:, None] == jnp.arange(experts, dtype=jnp.int32)[None, :]).astype(jnp.int32)
    rank = jnp.sum((jnp.cumsum(onehot, 0) - onehot) * onehot, 1)
    target = jnp.sum(onehot * expert_slot[None, :], 1)
    flat = (target * cap + rank).reshape(tok_rows, top)

    rows_j = jnp.arange(slots, dtype=jnp.int32)
    pick = jnp.any(flat[None, :, :] == rows_j[:, None, None], axis=2).astype(jnp.bfloat16)
    lanes = 128
    sub = width // lanes
    tokens_rel = _blocks(tokens, src_blk).reshape(tok_rows, sub, lanes)
    send = jnp.einsum("st,trl->srl", pick, tokens_rel, preferred_element_type=jnp.float32)
    send = send.astype(jnp.bfloat16).reshape(n_ep, cap * sub, lanes)
    send = lax.optimization_barrier((send, gate_cross))[0]
    received = lax.all_to_all(send, "ep", 0, 0, tiled=True)
    received = received.reshape(slots, width)

    gate = jnp.dot(received, wg, preferred_element_type=jnp.float32)
    up = jnp.dot(received, wu, preferred_element_type=jnp.float32)
    hidden = (jax.nn.silu(gate) * up).astype(jnp.bfloat16)
    wd = jnp.concatenate(_dp_parts(down_shard, after=lambda: hidden), axis=1)
    expert_out = jnp.dot(hidden, wd, preferred_element_type=jnp.float32).astype(jnp.bfloat16)

    expert_out = expert_out.reshape(n_ep, cap * sub, lanes)
    returned = lax.all_to_all(expert_out, "ep", 0, 0, tiled=True)
    returned = returned.reshape(slots, sub, lanes)

    hit = flat[:, :, None] == rows_j[None, None, :]
    weights = jnp.sum(jnp.where(hit, gate_scales[:, :, None], 0.0), axis=1)
    w_hi32 = lax.reduce_precision(weights, exponent_bits=8, mantissa_bits=7)
    w_hi = w_hi32.astype(jnp.bfloat16)
    w_lo = (weights - w_hi32).astype(jnp.bfloat16)
    both = jnp.einsum("ts,srl->trl", jnp.concatenate([w_hi, w_lo], axis=0), returned,
                      preferred_element_type=jnp.float32)
    mixed = both[:tok_rows] + both[tok_rows:]
    return _blocks(mixed.astype(jnp.bfloat16).reshape(tok_rows, width), out_blk)


def solution(mesh):
    in_specs = (
        P(("dp", "ep"), None),
        P(("dp", "ep"), None),
        P(("dp", "ep"), None),
        P(),
        P("ep", "dp", None),
        P("ep", "dp", None),
        P("ep", None, "dp"),
    )
    out_specs = P(("dp", "ep"), None)
    return jax.shard_map(local, mesh=mesh, in_specs=in_specs, out_specs=out_specs, check_vma=False)
```

```python
import jax
import jax.numpy as jnp
from jax import lax
from jax.sharding import PartitionSpec as P

C = 13
OFFS = (0, 2, 1, 3)


def _perm(n, m):
    return [(i, i ^ m) for i in range(n)]


def _dp_parts(w, after=None):
    n = lax.axis_size("dp")
    cross = lax.ppermute(w, "dp", _perm(n, 2))
    near = lax.ppermute(w, "dp", _perm(n, 1))
    relay = cross if after is None else lax.optimization_barrier((cross, after()))[0]
    far = lax.ppermute(relay, "dp", _perm(n, 1))
    return [w, cross, near, far]


def _blocks(x, idx):
    rows, width = x.shape
    nb = idx.shape[0]
    return jnp.take(x.reshape(rows, nb, width // nb), idx, axis=1).reshape(rows, width)


def local(tokens, expert_ids, gate_scales, expert_slot, gate_weight, up_weight, down_weight):
    tok_rows, width = tokens.shape
    top = expert_ids.shape[1]
    experts = expert_slot.shape[0]
    n_ep = lax.axis_size("ep")
    n_dp = lax.axis_size("dp")
    assert n_dp == len(OFFS) and gate_weight.shape[0] == 1 and experts == n_ep
    cap = C
    slots = experts * cap

    half = gate_weight.shape[1] // 2
    wg_a = _dp_parts(gate_weight[0, :half])
    gate_cross = wg_a[1]
    wg_b = _dp_parts(lax.optimization_barrier((gate_weight[0, half:], gate_cross))[0])
    up_shard = lax.optimization_barrier((up_weight[0], wg_b[1]))[0]
    wu = _dp_parts(up_shard)
    wg = jnp.concatenate([x for pair in zip(wg_a, wg_b) for x in pair], axis=0)
    down_shard = lax.optimization_barrier((down_weight[0], wu[1]))[0]
    wu = jnp.concatenate(wu, axis=0)

    d = lax.axis_index("dp")
    offs = jnp.array(OFFS, jnp.int32)
    src_blk = d ^ offs
    inv = jnp.argsort(offs).astype(jnp.int32)
    out_blk = inv[d ^ jnp.arange(n_dp, dtype=jnp.int32)]

    ids = expert_ids.reshape(-1)
    onehot = (ids[:, None] == jnp.arange(experts, dtype=jnp.int32)[None, :]).astype(jnp.int32)
    rank = jnp.sum((jnp.cumsum(onehot, 0) - onehot) * onehot, 1)
    target = jnp.sum(onehot * expert_slot[None, :], 1)
    flat = (target * cap + rank).reshape(tok_rows, top)

    rows_j = jnp.arange(slots, dtype=jnp.int32)
    pick = jnp.any(flat[None, :, :] == rows_j[:, None, None], axis=2).astype(jnp.bfloat16)
    lanes = 128
    sub = width // lanes
    tokens_rel = _blocks(tokens, src_blk).reshape(tok_rows, sub, lanes)
    send = jnp.einsum("st,trl->srl", pick, tokens_rel, preferred_element_type=jnp.float32)
    send = send.astype(jnp.bfloat16).reshape(n_ep, cap * sub, lanes)
    send = lax.optimization_barrier((send, gate_cross))[0]
    received = lax.all_to_all(send, "ep", 0, 0, tiled=True)
    received = received.reshape(slots, width)

    gate = jnp.dot(received, wg, preferred_element_type=jnp.float32)
    up = jnp.dot(received, wu, preferred_element_type=jnp.float32)
    hidden = (jax.nn.silu(gate) * up).astype(jnp.bfloat16)
    wd = jnp.concatenate(_dp_parts(down_shard, after=lambda: hidden), axis=1)
    expert_out = jnp.dot(hidden, wd, preferred_element_type=jnp.float32).astype(jnp.bfloat16)

    expert_out = expert_out.reshape(n_ep, cap * sub, lanes)
    returned = lax.all_to_all(expert_out, "ep", 0, 0, tiled=True)
    returned = returned.reshape(slots, sub, lanes)

    hit = flat[:, :, None] == rows_j[None, None, :]
    weights = jnp.sum(jnp.where(hit, gate_scales[:, :, None], 0.0), axis=1)
    w_hi32 = lax.reduce_precision(weights, exponent_bits=8, mantissa_bits=7)
    w_hi = w_hi32.astype(jnp.bfloat16)
    w_lo = (weights - w_hi32).astype(jnp.bfloat16)
    both = jnp.einsum("ts,srl->trl", jnp.concatenate([w_hi, w_lo], axis=0), returned,
                      preferred_element_type=jnp.float32)
    mixed = both[:tok_rows] + both[tok_rows:]
    return _blocks(mixed.astype(jnp.bfloat16).reshape(tok_rows, width), out_blk)


def solution(mesh):
    in_specs = (
        P(("dp", "ep"), None),
        P(("dp", "ep"), None),
        P(("dp", "ep"), None),
        P(),
        P("ep", "dp", None),
        P("ep", "dp", None),
        P("ep", None, "dp"),
    )
    out_specs = P(("dp", "ep"), None)
    return jax.shard_map(local, mesh=mesh, in_specs=in_specs, out_specs=out_specs, check_vma=False)
```

```python
import jax
import jax.numpy as jnp
from jax import lax
from jax.sharding import PartitionSpec as P

C = 13
OFFS = (0, 2, 1, 3)


def _perm(n, m):
    return [(i, i ^ m) for i in range(n)]


def _dp_parts(w, after=None):
    n = lax.axis_size("dp")
    cross = lax.ppermute(w, "dp", _perm(n, 2))
    near = lax.ppermute(w, "dp", _perm(n, 1))
    relay = cross if after is None else lax.optimization_barrier((cross, after()))[0]
    far = lax.ppermute(relay, "dp", _perm(n, 1))
    return [w, cross, near, far]


def _blocks(x, idx):
    rows, width = x.shape
    nb = idx.shape[0]
    return jnp.take(x.reshape(rows, nb, width // nb), idx, axis=1).reshape(rows, width)


def local(tokens, expert_ids, gate_scales, expert_slot, gate_weight, up_weight, down_weight):
    tok_rows, width = tokens.shape
    top = expert_ids.shape[1]
    experts = expert_slot.shape[0]
    n_ep = lax.axis_size("ep")
    n_dp = lax.axis_size("dp")
    assert n_dp == len(OFFS) and gate_weight.shape[0] == 1 and experts == n_ep
    cap = C
    slots = experts * cap

    wg = _dp_parts(gate_weight[0])
    up_shard = lax.optimization_barrier((up_weight[0], wg[1]))[0]
    wu = _dp_parts(up_shard)
    gate_cross = wg[1]
    wg = jnp.concatenate(wg, axis=0)
    down_shard = lax.optimization_barrier((down_weight[0], wu[1]))[0]
    wu = jnp.concatenate(wu, axis=0)

    d = lax.axis_index("dp")
    offs = jnp.array(OFFS, jnp.int32)
    src_blk = d ^ offs
    inv = jnp.argsort(offs).astype(jnp.int32)
    out_blk = inv[d ^ jnp.arange(n_dp, dtype=jnp.int32)]

    ids = expert_ids.reshape(-1)
    onehot = (ids[:, None] == jnp.arange(experts, dtype=jnp.int32)[None, :]).astype(jnp.int32)
    rank = jnp.sum((jnp.cumsum(onehot, 0) - onehot) * onehot, 1)
    target = jnp.sum(onehot * expert_slot[None, :], 1)
    flat = (target * cap + rank).reshape(tok_rows, top)

    rows_j = jnp.arange(slots, dtype=jnp.int32)
    pick = jnp.any(flat[None, :, :] == rows_j[:, None, None], axis=2).astype(jnp.bfloat16)
    lanes = 128
    sub = width // lanes
    tokens_rel = _blocks(tokens, src_blk).reshape(tok_rows, sub, lanes)
    send = jnp.einsum("st,trl->srl", pick, tokens_rel, preferred_element_type=jnp.float32)
    send = send.astype(jnp.bfloat16).reshape(n_ep, cap * sub, lanes)
    send = lax.optimization_barrier((send, gate_cross))[0]
    received = lax.all_to_all(send, "ep", 0, 0, tiled=True)
    received = received.reshape(slots, width)

    gate = jnp.dot(received, wg, preferred_element_type=jnp.float32)
    up = jnp.dot(received, wu, preferred_element_type=jnp.float32)
    hidden = (jax.nn.silu(gate) * up).astype(jnp.bfloat16)
    wd = _dp_parts(down_shard, after=lambda: hidden)
    first = jnp.dot(hidden, jnp.concatenate(wd[:3], axis=1), preferred_element_type=jnp.float32)
    last = jnp.dot(hidden, wd[3], preferred_element_type=jnp.float32)
    expert_out = jnp.concatenate([first, last], axis=1).astype(jnp.bfloat16)

    expert_out = expert_out.reshape(n_ep, cap * sub, lanes)
    returned = lax.all_to_all(expert_out, "ep", 0, 0, tiled=True)
    returned = returned.reshape(slots, sub, lanes)

    hit = flat[:, :, None] == rows_j[None, None, :]
    weights = jnp.sum(jnp.where(hit, gate_scales[:, :, None], 0.0), axis=1)
    w_hi32 = lax.reduce_precision(weights, exponent_bits=8, mantissa_bits=7)
    w_hi = w_hi32.astype(jnp.bfloat16)
    w_lo = (weights - w_hi32).astype(jnp.bfloat16)
    both = jnp.einsum("ts,srl->trl", jnp.concatenate([w_hi, w_lo], axis=0), returned,
                      preferred_element_type=jnp.float32)
    mixed = both[:tok_rows] + both[tok_rows:]
    return _blocks(mixed.astype(jnp.bfloat16).reshape(tok_rows, width), out_blk)


def solution(mesh):
    in_specs = (
        P(("dp", "ep"), None),
        P(("dp", "ep"), None),
        P(("dp", "ep"), None),
        P(),
        P("ep", "dp", None),
        P("ep", "dp", None),
        P("ep", None, "dp"),
    )
    out_specs = P(("dp", "ep"), None)
    return jax.shard_map(local, mesh=mesh, in_specs=in_specs, out_specs=out_specs, check_vma=False)
```

```python
import jax
import jax.numpy as jnp
from jax import lax
from jax.sharding import PartitionSpec as P

C = 13
OFFS = (0, 2, 1, 3)


def _perm(n, m):
    return [(i, i ^ m) for i in range(n)]


def _dp_parts(w, after=None):
    n = lax.axis_size("dp")
    cross = lax.ppermute(w, "dp", _perm(n, 2))
    near = lax.ppermute(w, "dp", _perm(n, 1))
    relay = cross if after is None else lax.optimization_barrier((cross, after()))[0]
    far = lax.ppermute(relay, "dp", _perm(n, 1))
    return [w, cross, near, far]


def _blocks(x, idx):
    rows, width = x.shape
    nb = idx.shape[0]
    return jnp.take(x.reshape(rows, nb, width // nb), idx, axis=1).reshape(rows, width)


def local(tokens, expert_ids, gate_scales, expert_slot, gate_weight, up_weight, down_weight):
    tok_rows, width = tokens.shape
    top = expert_ids.shape[1]
    experts = expert_slot.shape[0]
    n_ep = lax.axis_size("ep")
    n_dp = lax.axis_size("dp")
    assert n_dp == len(OFFS) and gate_weight.shape[0] == 1 and experts == n_ep
    cap = C
    slots = experts * cap

    wg = _dp_parts(gate_weight[0])
    up_shard = lax.optimization_barrier((up_weight[0], wg[1]))[0]
    wu = _dp_parts(up_shard)
    gate_cross = wg[1]
    wg = jnp.concatenate(wg, axis=0)
    down_shard = lax.optimization_barrier((down_weight[0], wu[1]))[0]
    wu = jnp.concatenate(wu, axis=0)

    d = lax.axis_index("dp")
    offs = jnp.array(OFFS, jnp.int32)
    src_blk = d ^ offs
    inv = jnp.argsort(offs).astype(jnp.int32)
    out_blk = inv[d ^ jnp.arange(n_dp, dtype=jnp.int32)]

    ids = expert_ids.reshape(-1)
    onehot = (ids[:, None] == jnp.arange(experts, dtype=jnp.int32)[None, :]).astype(jnp.int32)
    rank = jnp.sum((jnp.cumsum(onehot, 0) - onehot) * onehot, 1)
    target = jnp.sum(onehot * expert_slot[None, :], 1)
    flat = (target * cap + rank).reshape(tok_rows, top)

    rows_j = jnp.arange(slots, dtype=jnp.int32)
    pick = jnp.any(flat[None, :, :] == rows_j[:, None, None], axis=2).astype(jnp.bfloat16)
    lanes = 128
    sub = width // lanes
    tokens_rel = _blocks(tokens, src_blk).reshape(tok_rows, sub, lanes)
    send = jnp.einsum("st,trl->srl", pick, tokens_rel, preferred_element_type=jnp.float32)
    send = send.astype(jnp.bfloat16).reshape(n_ep, cap * sub, lanes)
    send = lax.optimization_barrier((send, gate_cross))[0]
    received = lax.all_to_all(send, "ep", 0, 0, tiled=True)
    received = received.reshape(slots, sub, lanes)

    gate = jnp.einsum("srl,rlf->sf", received, wg.reshape(sub, lanes, -1), preferred_element_type=jnp.float32)
    up = jnp.einsum("srl,rlf->sf", received, wu.reshape(sub, lanes, -1), preferred_element_type=jnp.float32)
    hidden = (jax.nn.silu(gate) * up).astype(jnp.bfloat16)
    wd = _dp_parts(down_shard, after=lambda: hidden)
    first = jnp.dot(hidden, jnp.concatenate(wd[:3], axis=1), preferred_element_type=jnp.float32)
    last = jnp.dot(hidden, wd[3], preferred_element_type=jnp.float32)
    expert_out = jnp.concatenate([first, last], axis=1).astype(jnp.bfloat16)

    expert_out = expert_out.reshape(n_ep, cap * sub, lanes)
    returned = lax.all_to_all(expert_out, "ep", 0, 0, tiled=True)
    returned = returned.reshape(slots, sub, lanes)

    hit = flat[:, :, None] == rows_j[None, None, :]
    weights = jnp.sum(jnp.where(hit, gate_scales[:, :, None], 0.0), axis=1)
    w_hi32 = lax.reduce_precision(weights, exponent_bits=8, mantissa_bits=7)
    w_hi = w_hi32.astype(jnp.bfloat16)
    w_lo = (weights - w_hi32).astype(jnp.bfloat16)
    both = jnp.einsum("ts,srl->trl", jnp.concatenate([w_hi, w_lo], axis=0), returned,
                      preferred_element_type=jnp.float32)
    mixed = both[:tok_rows] + both[tok_rows:]
    return _blocks(mixed.astype(jnp.bfloat16).reshape(tok_rows, width), out_blk)


def solution(mesh):
    in_specs = (
        P(("dp", "ep"), None),
        P(("dp", "ep"), None),
        P(("dp", "ep"), None),
        P(),
        P("ep", "dp", None),
        P("ep", "dp", None),
        P("ep", None, "dp"),
    )
    out_specs = P(("dp", "ep"), None)
    return jax.shard_map(local, mesh=mesh, in_specs=in_specs, out_specs=out_specs, check_vma=False)
```
